256 devices in a mesh: rep: 32 (over z, y_hi, core), tp: 8 (over x, y_lo).
Axes of the slice: x: 4, y: 4 (y_hi: 2, y_lo: 2; y = y_hi * 2 + y_lo), z: 8, core: 2. Of those that a mesh axis runs over, the one named last changes fastest.
Arguments:
- acts: bfloat16 [32, 1024, 4096], P('rep', 'tp'), may hold values from -6 to 6
- weights: bfloat16 [32, 4096, 4096], P('rep', None, 'tp'), may hold values from -6 to 6
- cotangent: bfloat16 [32, 1024, 4096], P('rep', None, 'tp'), may hold values from -6 to 6
- start_factors: float32 [4096, 32], replicated, may hold values from -6 to 6
Outputs:
- projected: bfloat16 [32, 1024, 4096], P('rep', None, 'tp')
- new_weights: bfloat16 [32, 4096, 4096], P('rep', None, 'tp')
The draws below stay inside these ranges and needn't reach their ends.
All inputs are finite; a program needn't handle non-finite values.
Results may differ from the reference program's by a relative error of at most 0.001.
Values may be sent and summed in bfloat16 or wider, within the bound.
No kernel may reach another device: no remote copies, remote signals or barrier semaphores. Data moves between devices by JAX's collectives and lax.ppermute only.
A program may use at most 128 MiB of HBM per device.

```python
import jax
import jax.numpy as jnp
from jax import lax

D = 4096
R = 32
STEPS = 3
TOKENS = 1024
REPS = 32


def block_scale(rng, extent, split, least, top_value):
    def one(dim, blocks):
        heights = jax.random.uniform(jax.random.fold_in(jax.random.fold_in(rng, 6), dim), (blocks,), jnp.float32, least / len(split), top_value / len(split))
        return jnp.repeat(jnp.exp(heights), extent[dim] // blocks).reshape((-1,) + (1,) * (len(extent) - dim - 1))

    loudness = one(*split[0])
    for cut in split[1:]:
        loudness = loudness * one(*cut)
    return loudness


def normal_values(own_key, dims, width, bound, pieces=(), kind=jnp.bfloat16):
    loudness = block_scale(own_key, dims, pieces, -0.22, 0.18) if pieces else 1.0
    result = jax.random.normal(own_key, dims, jnp.float32) * width * loudness
    return jnp.minimum(jnp.maximum(result, -bound), bound).astype(kind)


def setup_inputs(seed: int = 0) -> dict:
    streams_of = jax.random.split(jax.random.key(seed), 5)
    acts = normal_values(streams_of[0], (REPS, TOKENS, D), 1.0, 6.0, ((0, 32), (1, 8)))
    weights = normal_values(streams_of[1], (REPS, D, D), 1.0, 6.0, ((0, 32), (2, 8)))
    cotangent = normal_values(streams_of[2], (REPS, TOKENS, D), 1.0, 6.0, ((0, 32), (2, 8)))
    start_factors = normal_values(streams_of[3], (D, R), 1.0, 6.0, (), jnp.float32)
    return dict(acts=acts, weights=weights, cotangent=cotangent, start_factors=start_factors)


HIGH = lax.Precision.HIGHEST

def reference(acts, weights, cotangent, start_factors):
    scale = D ** (-0.5)

    def forward(pair):
        return (jnp.dot(pair[0].astype(jnp.float32), pair[1].astype(jnp.float32), preferred_element_type=jnp.float32) * scale).astype(jnp.bfloat16)
    projected = lax.map(forward, (acts, weights))

    def stepped(triple):
        grad = lax.dot_general(triple[0].astype(jnp.float32), triple[2].astype(jnp.float32), (((0,), (0,)), ((), ())), preferred_element_type=jnp.float32)
        return triple[1].astype(jnp.float32) - 0.5 * scale * grad
    current = lax.map(stepped, (acts, weights, cotangent))
    index = jnp.arange(REPS, dtype=jnp.int32)
    for step in range(STEPS):
        partner = jnp.bitwise_xor(index, jnp.int32(1 << step))
        side = jnp.einsum('rio,ik->rok', current, start_factors, precision=HIGH)
        diff = side - side[partner]
        gram = jnp.einsum('rok,rol->rkl', diff, diff, precision=HIGH)
        lower = jnp.linalg.cholesky(gram)
        solved = jax.scipy.linalg.solve_triangular(lower, jnp.transpose(diff, (0, 2, 1)), lower=True)
        ortho = jnp.transpose(solved, (0, 2, 1))
        local = jnp.einsum('rio,rok->rik', current, ortho, precision=HIGH)
        back = local + local[partner]
        current = current - 0.5 * jnp.einsum('rik,rok->rio', back, ortho, precision=HIGH)
    return (projected, current.astype(jnp.bfloat16))
```

```python
import numpy as np
import jax
import jax.numpy as jnp
from jax import lax
from jax.sharding import Mesh, PartitionSpec as P

D = 4096
STEPS = 3


HIGH = lax.Precision.HIGHEST
F32 = jnp.float32


def swap(block, axis):
    return lax.ppermute(block, axis, [(0, 1), (1, 0)])


def tp_perm(count, fn):
    return [(t, fn(t)) for t in range(count)]


def gather_tokens(own, count):
    if count != 8:
        whole = lax.all_gather(own, "tp", axis=0, tiled=False)
        return [whole[k] for k in range(count)], None
    nx = count // 2

    def shift(d):
        return tp_perm(count, lambda t: ((t // 2 + d) % nx) * 2 + t % 2)

    rows = own.shape[0]
    h = rows // 2
    a_y = lax.ppermute(own, "tp", tp_perm(count, lambda t: t ^ 1))
    a_m = lax.ppermute(own, "tp", shift(1))
    a_p = lax.ppermute(own, "tp", shift(-1))
    r_m = lax.ppermute(jnp.concatenate([a_y, a_m[:h]]), "tp", shift(1))
    r_p = lax.ppermute(jnp.concatenate([a_y, a_p[h:]]), "tp", shift(-1))
    c_m = lax.ppermute(r_m[:h], "tp", shift(1))
    c_p = lax.ppermute(r_p[h:rows], "tp", shift(-1))
    far = jnp.concatenate([r_m[rows:], r_p[rows:]])
    far_y = jnp.concatenate([c_m, c_p])
    return [own, a_y, a_p, r_p[:rows], far, far_y, a_m, r_m[:rows]], nx


def allreduce(parts, pair_axis, count):
    parts = [p + swap(p, pair_axis) for p in parts]
    bit = 1
    while bit < count:
        perm = tp_perm(count, lambda t, b=bit: t ^ b)
        parts = [p + lax.ppermute(p, "tp", perm) for p in parts]
        bit *= 2
    return parts


def shards(acts, weights, cotangent, start_factors):
    scale = D ** (-0.5)
    count = lax.axis_size("tp")
    weight_part = weights[0]
    grad_out = cotangent[0]
    rows = acts.shape[1]
    blocks, nx = gather_tokens(acts[0], count)
    t = lax.axis_index("tp")
    if nx is None:
        order = jnp.arange(count)
    else:
        k = jnp.arange(count)
        order = ((t // 2 + k // 2) % nx) * 2 + ((t % 2) ^ (k % 2))
    rel = jnp.concatenate(blocks)
    out_rel = jnp.dot(rel, weight_part, preferred_element_type=F32) * scale
    out_rel = out_rel.astype(jnp.bfloat16).reshape(count, rows, -1)
    inverse = jnp.zeros((count,), jnp.int32).at[order].set(jnp.arange(count, dtype=jnp.int32))
    projected = jnp.take(out_rel, inverse, axis=0).reshape(count * rows, -1)[None]
    grad_rel = jnp.take(grad_out.reshape(count, rows, -1), order, axis=0).reshape(count * rows, -1)
    grad = lax.dot_general(rel, grad_rel, (((0,), (0,)), ((), ())), preferred_element_type=F32)
    current = weight_part.astype(F32) - 0.5 * scale * grad
    side = lax.dot_general(current, start_factors, (((0,), (0,)), ((), ())), precision=HIGH)
    backs, orthos = [], []
    eye = jnp.eye(start_factors.shape[1], dtype=F32)
    for step in range(STEPS):
        axis = f"b{step}"
        diff = side - swap(side, axis)
        gram = jnp.dot(diff.T, diff, precision=HIGH)
        mixed = lax.dot_general(diff, current, (((0,), (1,)), ((), ())), precision=HIGH)
        for back_t, ortho_t in zip(backs, orthos):
            inner = jnp.dot(ortho_t, diff, precision=HIGH)
            mixed = mixed - 0.5 * lax.dot_general(inner, back_t, (((0,), (0,)), ((), ())), precision=HIGH)
        gram, mixed = allreduce([gram, mixed], axis, count)
        lower = jnp.linalg.cholesky(0.5 * gram)
        inv = jax.scipy.linalg.solve_triangular(lower, eye, lower=True)
        back_t = jnp.dot(inv, mixed, precision=HIGH)
        ortho_t = jnp.dot(inv, diff.T, precision=HIGH)
        backs.append(back_t)
        orthos.append(ortho_t)
        if step + 1 < STEPS:
            proj = jnp.dot(back_t, start_factors, precision=HIGH)
            side = side - 0.5 * lax.dot_general(ortho_t, proj, (((0,), (0,)), ((), ())), precision=HIGH)
    back_all = jnp.concatenate(backs)
    ortho_all = jnp.concatenate(orthos)
    update = lax.dot_general(back_all, ortho_all, (((0,), (0,)), ((), ())), precision=HIGH)
    new = current - 0.5 * update
    return (projected, new.astype(jnp.bfloat16)[None])


def solution(mesh):
    reps = mesh.shape["rep"]
    high = reps >> STEPS
    names = ("rh",) + tuple(f"b{s}" for s in reversed(range(STEPS)))
    devices = np.asarray(mesh.devices).reshape((high,) + (2,) * STEPS + (mesh.shape["tp"],))
    split = Mesh(devices, names + ("tp",))
    rep = names
    in_specs = (P(rep, "tp", None), P(rep, None, "tp"), P(rep, None, "tp"), P())
    out_specs = (P(rep, None, "tp"), P(rep, None, "tp"))
    return jax.shard_map(shards, mesh=split, in_specs=in_specs, out_specs=out_specs, check_vma=False)
```

```python
import numpy as np
import jax
import jax.numpy as jnp
from jax import lax
from jax.sharding import Mesh, PartitionSpec as P

D = 4096
STEPS = 3


HIGH = lax.Precision.HIGHEST
FAST = lax.Precision.HIGH
F32 = jnp.float32


def swap(block, axis):
    return lax.ppermute(block, axis, [(0, 1), (1, 0)])


def tp_perm(count, fn):
    return [(t, fn(t)) for t in range(count)]


def gather_tokens(own, count):
    if count != 8:
        whole = lax.all_gather(own, "tp", axis=0, tiled=False)
        return [whole[k] for k in range(count)], None
    nx = count // 2

    def shift(d):
        return tp_perm(count, lambda t: ((t // 2 + d) % nx) * 2 + t % 2)

    h = own.shape[0] // 2
    pair = tp_perm(count, lambda t: t ^ 1)
    a_y = lax.ppermute(own, "tp", pair)
    a_m = lax.ppermute(own, "tp", shift(1))
    a_p = lax.ppermute(own, "tp", shift(-1))
    b_m = lax.ppermute(a_y, "tp", shift(1))
    b_p = lax.ppermute(a_p, "tp", shift(-1))
    b_y = lax.ppermute(a_p, "tp", pair)
    c_y = lax.ppermute(b_p[:h], "tp", pair)
    c_p = lax.ppermute(b_y[h:], "tp", shift(-1))
    return [own, a_y, a_p, b_y, b_p, jnp.concatenate([c_y, c_p]), a_m, b_m], nx


def allreduce(parts, pair_axis, count):
    parts = [p + swap(p, pair_axis) for p in parts]
    bit = 1
    while bit < count:
        perm = tp_perm(count, lambda t, b=bit: t ^ b)
        parts = [p + lax.ppermute(p, "tp", perm) for p in parts]
        bit *= 2
    return parts


def shards(acts, weights, cotangent, start_factors):
    scale = D ** (-0.5)
    count = lax.axis_size("tp")
    weight_part = weights[0]
    grad_out = cotangent[0]
    rows = acts.shape[1]
    blocks, nx = gather_tokens(acts[0], count)
    t = lax.axis_index("tp")
    if nx is None:
        order = jnp.arange(count)
    else:
        k = jnp.arange(count)
        order = ((t // 2 + k // 2) % nx) * 2 + ((t % 2) ^ (k % 2))
    rel = jnp.concatenate(blocks)
    out_rel = jnp.dot(rel, weight_part, preferred_element_type=F32) * scale
    out_rel = out_rel.astype(jnp.bfloat16).reshape(count, rows, -1)
    inverse = jnp.zeros((count,), jnp.int32).at[order].set(jnp.arange(count, dtype=jnp.int32))
    projected = jnp.take(out_rel, inverse, axis=0).reshape(count * rows, -1)[None]
    grad_rel = jnp.take(grad_out.reshape(count, rows, -1), order, axis=0).reshape(count * rows, -1)
    grad = lax.dot_general(rel, grad_rel, (((0,), (0,)), ((), ())), preferred_element_type=F32)
    current = weight_part.astype(F32) - 0.5 * scale * grad
    side = lax.dot_general(current, start_factors, (((0,), (0,)), ((), ())), precision=FAST)
    backs, orthos = [], []
    eye = jnp.eye(start_factors.shape[1], dtype=F32)
    for step in range(STEPS):
        axis = f"b{step}"
        diff = side - swap(side, axis)
        gram = jnp.dot(diff.T, diff, precision=HIGH)
        mixed = lax.dot_general(diff, current, (((0,), (1,)), ((), ())), precision=FAST)
        for back_t, ortho_t in zip(backs, orthos):
            inner = jnp.dot(ortho_t, diff, precision=HIGH)
            mixed = mixed - 0.5 * lax.dot_general(inner, back_t, (((0,), (0,)), ((), ())), precision=HIGH)
        width = mixed.shape[0]
        packed = jnp.concatenate([jnp.pad(gram, ((0, 0), (0, 128 - width))), mixed], axis=1)
        (packed,) = allreduce([packed], axis, count)
        gram, mixed = packed[:, :width], packed[:, 128:]
        lower = jnp.linalg.cholesky(0.5 * gram)
        inv = jax.scipy.linalg.solve_triangular(lower, eye, lower=True)
        back_t = jnp.dot(inv, mixed, precision=HIGH)
        ortho_t = jnp.dot(inv, diff.T, precision=HIGH)
        backs.append(back_t)
        orthos.append(ortho_t)
        if step + 1 < STEPS:
            proj = jnp.dot(back_t, start_factors, precision=HIGH)
            side = side - 0.5 * lax.dot_general(ortho_t, proj, (((0,), (0,)), ((), ())), precision=HIGH)
    back_all = jnp.concatenate(backs)
    ortho_all = jnp.concatenate(orthos)
    update = lax.dot_general(back_all, ortho_all, (((0,), (0,)), ((), ())), precision=FAST)
    new = current - 0.5 * update
    return (projected, new.astype(jnp.bfloat16)[None])


def solution(mesh):
    reps = mesh.shape["rep"]
    high = reps >> STEPS
    names = ("rh",) + tuple(f"b{s}" for s in reversed(range(STEPS)))
    devices = np.asarray(mesh.devices).reshape((high,) + (2,) * STEPS + (mesh.shape["tp"],))
    split = Mesh(devices, names + ("tp",))
    rep = names
    in_specs = (P(rep, "tp", None), P(rep, None, "tp"), P(rep, None, "tp"), P())
    out_specs = (P(rep, None, "tp"), P(rep, None, "tp"))
    return jax.shard_map(shards, mesh=split, in_specs=in_specs, out_specs=out_specs, check_vma=False)
```

```python
import numpy as np
import jax
import jax.numpy as jnp
from jax import lax
from jax.sharding import Mesh, PartitionSpec as P

D = 4096
STEPS = 3


HIGH = lax.Precision.HIGHEST
FAST = lax.Precision.HIGH
F32 = jnp.float32


def swap(block, axis):
    return lax.ppermute(block, axis, [(0, 1), (1, 0)])


def tp_perm(count, fn):
    return [(t, fn(t)) for t in range(count)]


def gather_tokens(own, count):
    if count != 8:
        whole = lax.all_gather(own, "tp", axis=0, tiled=False)
        return [whole[k] for k in range(count)], None
    nx = count // 2

    def shift(d):
        return tp_perm(count, lambda t: ((t // 2 + d) % nx) * 2 + t % 2)

    h = own.shape[0] // 2
    pair = tp_perm(count, lambda t: t ^ 1)
    a_y = lax.ppermute(own, "tp", pair)
    a_m = lax.ppermute(own, "tp", shift(1))
    a_p = lax.ppermute(own, "tp", shift(-1))
    b_m = lax.ppermute(a_y, "tp", shift(1))
    b_p = lax.ppermute(a_p, "tp", shift(-1))
    b_y = lax.ppermute(a_p, "tp", pair)
    c_y = lax.ppermute(b_p[:h], "tp", pair)
    c_p = lax.ppermute(b_y[h:], "tp", shift(-1))
    return [own, a_y, a_p, b_y, b_p, jnp.concatenate([c_y, c_p]), a_m, b_m], nx


def allreduce(parts, pair_axis, count):
    parts = [p + swap(p, pair_axis) for p in parts]
    bit = 1
    while bit < count:
        perm = tp_perm(count, lambda t, b=bit: t ^ b)
        parts = [p + lax.ppermute(p, "tp", perm) for p in parts]
        bit *= 2
    return parts


def halving_allreduce(buf, pair_axis, count):
    t = lax.axis_index("tp")
    stages = [(pair_axis, lax.axis_index(pair_axis), [(0, 1), (1, 0)])]
    bit = 1
    while bit < count:
        stages.append(("tp", (t // bit) % 2, tp_perm(count, lambda u, b=bit: u ^ b)))
        bit *= 2
    for axis, v, perm in stages:
        half = buf.shape[0] // 2
        keep = lax.dynamic_slice_in_dim(buf, v * half, half, 0)
        give = lax.dynamic_slice_in_dim(buf, (1 - v) * half, half, 0)
        buf = keep + lax.ppermute(give, axis, perm)
    for axis, v, perm in reversed(stages):
        other = lax.ppermute(buf, axis, perm)
        buf = jnp.where(v == 1, jnp.concatenate([other, buf]), jnp.concatenate([buf, other]))
    return buf


def shards(acts, weights, cotangent, start_factors):
    scale = D ** (-0.5)
    count = lax.axis_size("tp")
    weight_part = weights[0]
    grad_out = cotangent[0]
    rows = acts.shape[1]
    blocks, nx = gather_tokens(acts[0], count)
    t = lax.axis_index("tp")
    if nx is None:
        order = jnp.arange(count)
    else:
        k = jnp.arange(count)
        order = ((t // 2 + k // 2) % nx) * 2 + ((t % 2) ^ (k % 2))
    rel = jnp.concatenate(blocks)
    out_rel = jnp.dot(rel, weight_part, preferred_element_type=F32) * scale
    out_rel = out_rel.astype(jnp.bfloat16).reshape(count, rows, -1)
    inverse = jnp.zeros((count,), jnp.int32).at[order].set(jnp.arange(count, dtype=jnp.int32))
    projected = jnp.take(out_rel, inverse, axis=0).reshape(count * rows, -1)[None]
    grad_rel = jnp.take(grad_out.reshape(count, rows, -1), order, axis=0).reshape(count * rows, -1)
    grad = lax.dot_general(rel, grad_rel, (((0,), (0,)), ((), ())), preferred_element_type=F32)
    current = weight_part.astype(F32) - 0.5 * scale * grad
    side = lax.dot_general(current, start_factors, (((0,), (0,)), ((), ())), precision=FAST)
    pieces = 2 * count
    current3 = current.reshape(pieces, -1, current.shape[1])
    factors3 = start_factors.reshape(pieces, -1, start_factors.shape[1])
    backs, orthos = [], []
    eye = jnp.eye(start_factors.shape[1], dtype=F32)
    for step in range(STEPS):
        axis = f"b{step}"
        diff = side - swap(side, axis)
        gram = jnp.dot(diff.T, diff, precision=HIGH)
        mixed = jnp.einsum("gio,ok->gki", current3, diff, precision=FAST)
        for back3, ortho_t in zip(backs, orthos):
            inner = jnp.dot(ortho_t, diff, precision=HIGH)
            mixed = mixed - 0.5 * jnp.einsum("lk,gli->gki", inner, back3, precision=HIGH)
        (gram,) = allreduce([gram], axis, count)
        mixed = halving_allreduce(mixed, axis, count)
        lower = jnp.linalg.cholesky(0.5 * gram)
        inv = jax.scipy.linalg.solve_triangular(lower, eye, lower=True)
        back3 = jnp.einsum("kl,gli->gki", inv, mixed, precision=HIGH)
        ortho_t = jnp.dot(inv, diff.T, precision=HIGH)
        backs.append(back3)
        orthos.append(ortho_t)
        if step + 1 < STEPS:
            proj = jnp.einsum("gki,gil->kl", back3, factors3, precision=HIGH)
            side = side - 0.5 * lax.dot_general(ortho_t, proj, (((0,), (0,)), ((), ())), precision=HIGH)
    back_all = jnp.concatenate(backs, axis=1)
    ortho_all = jnp.concatenate(orthos)
    update = jnp.einsum("gki,ko->gio", back_all, ortho_all, precision=FAST).reshape(current.shape)
    new = current - 0.5 * update
    return (projected, new.astype(jnp.bfloat16)[None])


def solution(mesh):
    reps = mesh.shape["rep"]
    high = reps >> STEPS
    names = ("rh",) + tuple(f"b{s}" for s in reversed(range(STEPS)))
    devices = np.asarray(mesh.devices).reshape((high,) + (2,) * STEPS + (mesh.shape["tp"],))
    split = Mesh(devices, names + ("tp",))
    rep = names
    in_specs = (P(rep, "tp", None), P(rep, None, "tp"), P(rep, None, "tp"), P())
    out_specs = (P(rep, None, "tp"), P(rep, None, "tp"))
    return jax.shard_map(shards, mesh=split, in_specs=in_specs, out_specs=out_specs, check_vma=False)
```

```python
import numpy as np
import jax
import jax.numpy as jnp
from jax import lax
from jax.sharding import Mesh, PartitionSpec as P

D = 4096
STEPS = 3


HIGH = lax.Precision.HIGHEST
FAST = lax.Precision.HIGH
F32 = jnp.float32


def swap(block, axis):
    return lax.ppermute(block, axis, [(0, 1), (1, 0)])


def tp_perm(count, fn):
    return [(t, fn(t)) for t in range(count)]


def gather_tokens(own, count):
    if count != 8:
        whole = lax.all_gather(own, "tp", axis=0, tiled=False)
        return [whole[k] for k in range(count)], None
    nx = count // 2

    def shift(d):
        return tp_perm(count, lambda t: ((t // 2 + d) % nx) * 2 + t % 2)

    h = own.shape[0] // 2
    pair = tp_perm(count, lambda t: t ^ 1)
    a_y = lax.ppermute(own, "tp", pair)
    a_m = lax.ppermute(own, "tp", shift(1))
    a_p = lax.ppermute(own, "tp", shift(-1))
    b_m = lax.ppermute(a_y, "tp", shift(1))
    b_p = lax.ppermute(a_p, "tp", shift(-1))
    b_y = lax.ppermute(a_p, "tp", pair)
    c_y = lax.ppermute(b_p[:h], "tp", pair)
    c_p = lax.ppermute(b_y[h:], "tp", shift(-1))
    return [own, a_y, a_p, b_y, b_p, jnp.concatenate([c_y, c_p]), a_m, b_m], nx


def allreduce(parts, pair_axis, count):
    parts = [p + swap(p, pair_axis) for p in parts]
    bit = 1
    while bit < count:
        perm = tp_perm(count, lambda t, b=bit: t ^ b)
        parts = [p + lax.ppermute(p, "tp", perm) for p in parts]
        bit *= 2
    return parts


def halving_allreduce(buf, pair_axis, count):
    t = lax.axis_index("tp")
    stages = [(pair_axis, lax.axis_index(pair_axis), [(0, 1), (1, 0)])]
    bit = 1
    while bit < count:
        stages.append(("tp", (t // bit) % 2, tp_perm(count, lambda u, b=bit: u ^ b)))
        bit *= 2
    for axis, v, perm in stages:
        half = buf.shape[0] // 2
        keep = lax.dynamic_slice_in_dim(buf, v * half, half, 0)
        give = lax.dynamic_slice_in_dim(buf, (1 - v) * half, half, 0)
        buf = keep + lax.ppermute(give, axis, perm)
    for axis, v, perm in reversed(stages):
        other = lax.ppermute(buf, axis, perm)
        buf = jnp.where(v == 1, jnp.concatenate([other, buf]), jnp.concatenate([buf, other]))
    return buf


def shards(acts, weights, cotangent, start_factors):
    scale = D ** (-0.5)
    count = lax.axis_size("tp")
    weight_part = weights[0]
    grad_out = cotangent[0]
    rows = acts.shape[1]
    blocks, nx = gather_tokens(acts[0], count)
    t = lax.axis_index("tp")
    if nx is None:
        order = jnp.arange(count)
    else:
        k = jnp.arange(count)
        order = ((t // 2 + k // 2) % nx) * 2 + ((t % 2) ^ (k % 2))
    grad_rel = jnp.take(grad_out.reshape(count, rows, -1), order, axis=0)
    groups = [(0, 1, 2, 6), (3, 4, 7), (5,)] if nx is not None else [tuple(range(count))]
    outs = [None] * count
    grad = None
    for group in groups:
        chunk = jnp.concatenate([blocks[k] for k in group])
        part = (jnp.dot(chunk, weight_part, preferred_element_type=F32) * scale).astype(jnp.bfloat16)
        for i, k in enumerate(group):
            outs[k] = part[i * rows:(i + 1) * rows]
        cot = jnp.concatenate([grad_rel[k] for k in group])
        term = lax.dot_general(chunk, cot, (((0,), (0,)), ((), ())), preferred_element_type=F32)
        grad = term if grad is None else grad + term
    out_rel = jnp.stack(outs)
    inverse = jnp.zeros((count,), jnp.int32).at[order].set(jnp.arange(count, dtype=jnp.int32))
    projected = jnp.take(out_rel, inverse, axis=0).reshape(count * rows, -1)[None]
    current = weight_part.astype(F32) - 0.5 * scale * grad
    side = lax.dot_general(current, start_factors, (((0,), (0,)), ((), ())), precision=FAST)
    pieces = 2 * count
    current3 = current.reshape(pieces, -1, current.shape[1])
    factors3 = start_factors.reshape(pieces, -1, start_factors.shape[1])
    backs, orthos = [], []
    eye = jnp.eye(start_factors.shape[1], dtype=F32)
    for step in range(STEPS):
        axis = f"b{step}"
        diff = side - swap(side, axis)
        gram = jnp.dot(diff.T, diff, precision=HIGH)
        mixed = jnp.einsum("gio,ok->gki", current3, diff, precision=FAST)
        for back3, ortho_t in zip(backs, orthos):
            inner = jnp.dot(ortho_t, diff, precision=HIGH)
            mixed = mixed - 0.5 * jnp.einsum("lk,gli->gki", inner, back3, precision=HIGH)
        (gram,) = allreduce([gram], axis, count)
        mixed = halving_allreduce(mixed, axis, count)
        lower = jnp.linalg.cholesky(0.5 * gram)
        inv = jax.scipy.linalg.solve_triangular(lower, eye, lower=True)
        back3 = jnp.einsum("kl,gli->gki", inv, mixed, precision=HIGH)
        ortho_t = jnp.dot(inv, diff.T, precision=HIGH)
        backs.append(back3)
        orthos.append(ortho_t)
        if step + 1 < STEPS:
            proj = jnp.einsum("gki,gil->kl", back3, factors3, precision=HIGH)
            side = side - 0.5 * lax.dot_general(ortho_t, proj, (((0,), (0,)), ((), ())), precision=HIGH)
    back_all = jnp.concatenate(backs, axis=1)
    ortho_all = jnp.concatenate(orthos)
    update = jnp.einsum("gki,ko->gio", back_all, ortho_all, precision=FAST).reshape(current.shape)
    new = current - 0.5 * update
    return (projected, new.astype(jnp.bfloat16)[None])


def solution(mesh):
    reps = mesh.shape["rep"]
    high = reps >> STEPS
    names = ("rh",) + tuple(f"b{s}" for s in reversed(range(STEPS)))
    devices = np.asarray(mesh.devices).reshape((high,) + (2,) * STEPS + (mesh.shape["tp"],))
    split = Mesh(devices, names + ("tp",))
    rep = names
    in_specs = (P(rep, "tp", None), P(rep, None, "tp"), P(rep, None, "tp"), P())
    out_specs = (P(rep, None, "tp"), P(rep, None, "tp"))
    return jax.shard_map(shards, mesh=split, in_specs=in_specs, out_specs=out_specs, check_vma=False)
```

```python
import numpy as np
import jax
import jax.numpy as jnp
from jax import lax
from jax.sharding import Mesh, PartitionSpec as P

D = 4096
STEPS = 3


HIGH = lax.Precision.HIGHEST
FAST = lax.Precision.HIGH
F32 = jnp.float32


def swap(block, axis):
    return lax.ppermute(block, axis, [(0, 1), (1, 0)])


def tp_perm(count, fn):
    return [(t, fn(t)) for t in range(count)]


def gather_tokens(own, count):
    if count != 8:
        whole = lax.all_gather(own, "tp", axis=0, tiled=False)
        return [whole[k] for k in range(count)], None
    nx = count // 2

    def shift(d):
        return tp_perm(count, lambda t: ((t // 2 + d) % nx) * 2 + t % 2)

    h = own.shape[0] // 2
    pair = tp_perm(count, lambda t: t ^ 1)
    a_y = lax.ppermute(own, "tp", pair)
    a_m = lax.ppermute(own, "tp", shift(1))
    a_p = lax.ppermute(own, "tp", shift(-1))
    b_m = lax.ppermute(a_y, "tp", shift(1))
    b_p = lax.ppermute(a_p, "tp", shift(-1))
    b_y = lax.ppermute(a_p, "tp", pair)
    c_y = lax.ppermute(b_p[:h], "tp", pair)
    c_p = lax.ppermute(b_y[h:], "tp", shift(-1))
    return [own, a_y, a_p, b_y, b_p, jnp.concatenate([c_y, c_p]), a_m, b_m], nx


def allreduce(parts, pair_axis, count):
    parts = [p + swap(p, pair_axis) for p in parts]
    bit = 1
    while bit < count:
        perm = tp_perm(count, lambda t, b=bit: t ^ b)
        parts = [p + lax.ppermute(p, "tp", perm) for p in parts]
        bit *= 2
    return parts


def halving_allreduce(keep, give, pair_axis, count):
    t = lax.axis_index("tp")
    stages = [(pair_axis, lax.axis_index(pair_axis), [(0, 1), (1, 0)])]
    bit = 1
    while bit < count:
        stages.append(("tp", (t // bit) % 2, tp_perm(count, lambda u, b=bit: u ^ b)))
        bit *= 2
    buf = keep + lax.ppermute(give, pair_axis, stages[0][2])
    for axis, v, perm in stages[1:]:
        half = buf.shape[0] // 2
        keep = lax.dynamic_slice_in_dim(buf, v * half, half, 0)
        give = lax.dynamic_slice_in_dim(buf, (1 - v) * half, half, 0)
        buf = keep + lax.ppermute(give, axis, perm)
    for axis, v, perm in reversed(stages):
        other = lax.ppermute(buf, axis, perm)
        buf = jnp.where(v == 1, jnp.concatenate([other, buf]), jnp.concatenate([buf, other]))
    return buf


def shards(acts, weights, cotangent, start_factors):
    scale = D ** (-0.5)
    count = lax.axis_size("tp")
    weight_part = weights[0]
    grad_out = cotangent[0]
    rows = acts.shape[1]
    blocks, nx = gather_tokens(acts[0], count)
    t = lax.axis_index("tp")
    if nx is None:
        order = jnp.arange(count)
    else:
        k = jnp.arange(count)
        order = ((t // 2 + k // 2) % nx) * 2 + ((t % 2) ^ (k % 2))
    grad_rel = jnp.take(grad_out.reshape(count, rows, -1), order, axis=0)
    groups = [(0, 1, 2, 6), (3, 4, 7), (5,)] if nx is not None else [tuple(range(count))]
    outs = [None] * count
    grad = None
    for group in groups:
        chunk = jnp.concatenate([blocks[k] for k in group])
        part = (jnp.dot(chunk, weight_part, preferred_element_type=F32) * scale).astype(jnp.bfloat16)
        for i, k in enumerate(group):
            outs[k] = part[i * rows:(i + 1) * rows]
        cot = jnp.concatenate([grad_rel[k] for k in group])
        term = lax.dot_general(chunk, cot, (((0,), (0,)), ((), ())), preferred_element_type=F32)
        grad = term if grad is None else grad + term
    out_rel = jnp.stack(outs)
    inverse = jnp.zeros((count,), jnp.int32).at[order].set(jnp.arange(count, dtype=jnp.int32))
    projected = jnp.take(out_rel, inverse, axis=0).reshape(count * rows, -1)[None]
    current = weight_part.astype(F32) - 0.5 * scale * grad
    side = lax.dot_general(current, start_factors, (((0,), (0,)), ((), ())), precision=FAST)
    pieces = 2 * count
    current3 = current.reshape(pieces, -1, current.shape[1])
    factors3 = start_factors.reshape(pieces, -1, start_factors.shape[1])
    backs, orthos = [], []
    eye = jnp.eye(start_factors.shape[1], dtype=F32)
    for step in range(STEPS):
        axis = f"b{step}"
        diff = side - swap(side, axis)
        gram = jnp.dot(diff.T, diff, precision=HIGH)
        v = lax.axis_index(axis)
        halves = []
        for start in ((1 - v) * (pieces // 2), v * (pieces // 2)):
            part = jnp.einsum("gio,ok->gki", lax.dynamic_slice_in_dim(current3, start, pieces // 2, 0), diff, precision=FAST)
            for back3, ortho_t in zip(backs, orthos):
                inner = jnp.dot(ortho_t, diff, precision=HIGH)
                back_half = lax.dynamic_slice_in_dim(back3, start, pieces // 2, 0)
                part = part - 0.5 * jnp.einsum("lk,gli->gki", inner, back_half, precision=HIGH)
            halves.append(part)
        (gram,) = allreduce([gram], axis, count)
        mixed = halving_allreduce(halves[1], halves[0], axis, count)
        lower = jnp.linalg.cholesky(0.5 * gram)
        inv = jax.scipy.linalg.solve_triangular(lower, eye, lower=True)
        back3 = jnp.einsum("kl,gli->gki", inv, mixed, precision=HIGH)
        ortho_t = jnp.dot(inv, diff.T, precision=HIGH)
        backs.append(back3)
        orthos.append(ortho_t)
        if step + 1 < STEPS:
            proj = jnp.einsum("gki,gil->kl", back3, factors3, precision=HIGH)
            side = side - 0.5 * lax.dot_general(ortho_t, proj, (((0,), (0,)), ((), ())), precision=HIGH)
    back_all = jnp.concatenate(backs, axis=1)
    back_all = jnp.transpose(back_all, (1, 0, 2)).reshape(back_all.shape[1], -1)
    ortho_all = jnp.concatenate(orthos)
    update = lax.dot_general(back_all, ortho_all, (((0,), (0,)), ((), ())), precision=FAST)
    new = current - 0.5 * update
    return (projected, new.astype(jnp.bfloat16)[None])


def solution(mesh):
    reps = mesh.shape["rep"]
    high = reps >> STEPS
    names = ("rh",) + tuple(f"b{s}" for s in reversed(range(STEPS)))
    devices = np.asarray(mesh.devices).reshape((high,) + (2,) * STEPS + (mesh.shape["tp"],))
    split = Mesh(devices, names + ("tp",))
    rep = names
    in_specs = (P(rep, "tp", None), P(rep, None, "tp"), P(rep, None, "tp"), P())
    out_specs = (P(rep, None, "tp"), P(rep, None, "tp"))
    return jax.shard_map(shards, mesh=split, in_specs=in_specs, out_specs=out_specs, check_vma=False)
```

```python
import numpy as np
import jax
import jax.numpy as jnp
from jax import lax
from jax.sharding import Mesh, PartitionSpec as P

D = 4096
STEPS = 3


HIGH = lax.Precision.HIGHEST
FAST = lax.Precision.HIGH
F32 = jnp.float32


def swap(block, axis):
    return lax.ppermute(block, axis, [(0, 1), (1, 0)])


def tp_perm(count, fn):
    return [(t, fn(t)) for t in range(count)]


def gather_tokens(own, count):
    if count != 8:
        whole = lax.all_gather(own, "tp", axis=0, tiled=False)
        return [whole[k] for k in range(count)], None
    nx = count // 2

    def shift(d):
        return tp_perm(count, lambda t: ((t // 2 + d) % nx) * 2 + t % 2)

    h = own.shape[0] // 2
    pair = tp_perm(count, lambda t: t ^ 1)
    a_y = lax.ppermute(own, "tp", pair)
    a_m = lax.ppermute(own, "tp", shift(1))
    a_p = lax.ppermute(own, "tp", shift(-1))
    b_m = lax.ppermute(a_y, "tp", shift(1))
    b_p = lax.ppermute(a_p, "tp", shift(-1))
    b_y = lax.ppermute(a_p, "tp", pair)
    c_y = lax.ppermute(b_p[:h], "tp", pair)
    c_p = lax.ppermute(b_y[h:], "tp", shift(-1))
    return [own, a_y, a_p, b_y, b_p, jnp.concatenate([c_y, c_p]), a_m, b_m], nx


def allreduce(parts, pair_axis, count):
    parts = [p + swap(p, pair_axis) for p in parts]
    bit = 1
    while bit < count:
        perm = tp_perm(count, lambda t, b=bit: t ^ b)
        parts = [p + lax.ppermute(p, "tp", perm) for p in parts]
        bit *= 2
    return parts


def halving_allreduce(keep, give, pair_axis, count, rows):
    t = lax.axis_index("tp")
    stages = [(pair_axis, lax.axis_index(pair_axis), [(0, 1), (1, 0)])]
    bit = 1
    while bit < count:
        stages.append(("tp", (t // bit) % 2, tp_perm(count, lambda u, b=bit: u ^ b)))
        bit *= 2
    buf = keep + lax.ppermute(give, pair_axis, stages[0][2])
    for axis, v, perm in stages[1:]:
        half = buf.shape[0] // 2
        keep = lax.dynamic_slice_in_dim(buf, v * half, half, 0)
        give = lax.dynamic_slice_in_dim(buf, (1 - v) * half, half, 0)
        buf = keep + lax.ppermute(give, axis, perm)
    extra = buf[0, rows:]
    buf = buf[:, :rows]
    for axis, v, perm in reversed(stages):
        other = lax.ppermute(buf, axis, perm)
        buf = jnp.where(v == 1, jnp.concatenate([other, buf]), jnp.concatenate([buf, other]))
    return buf, extra


def shards(acts, weights, cotangent, start_factors):
    scale = D ** (-0.5)
    count = lax.axis_size("tp")
    weight_part = weights[0]
    grad_out = cotangent[0]
    rows = acts.shape[1]
    blocks, nx = gather_tokens(acts[0], count)
    t = lax.axis_index("tp")
    if nx is None:
        order = jnp.arange(count)
    else:
        k = jnp.arange(count)
        order = ((t // 2 + k // 2) % nx) * 2 + ((t % 2) ^ (k % 2))
    grad_rel = jnp.take(grad_out.reshape(count, rows, -1), order, axis=0)
    groups = [(0, 1, 2, 6), (3, 4, 7), (5,)] if nx is not None else [tuple(range(count))]
    outs = [None] * count
    grad = None
    for group in groups:
        chunk = jnp.concatenate([blocks[k] for k in group])
        part = (jnp.dot(chunk, weight_part, preferred_element_type=F32) * scale).astype(jnp.bfloat16)
        for i, k in enumerate(group):
            outs[k] = part[i * rows:(i + 1) * rows]
        cot = jnp.concatenate([grad_rel[k] for k in group])
        term = lax.dot_general(chunk, cot, (((0,), (0,)), ((), ())), preferred_element_type=F32)
        grad = term if grad is None else grad + term
    out_rel = jnp.stack(outs)
    inverse = jnp.zeros((count,), jnp.int32).at[order].set(jnp.arange(count, dtype=jnp.int32))
    projected = jnp.take(out_rel, inverse, axis=0).reshape(count * rows, -1)[None]
    current = weight_part.astype(F32) - 0.5 * scale * grad
    side = lax.dot_general(current, start_factors, (((0,), (0,)), ((), ())), precision=FAST)
    pieces = 2 * count
    current3 = current.reshape(pieces, -1, current.shape[1])
    factors3 = start_factors.reshape(pieces, -1, start_factors.shape[1])
    backs, orthos = [], []
    eye = jnp.eye(start_factors.shape[1], dtype=F32)
    for step in range(STEPS):
        axis = f"b{step}"
        diff = side - swap(side, axis)
        gram = jnp.dot(diff.T, diff, precision=HIGH)
        v = lax.axis_index(axis)
        halves = []
        for start in ((1 - v) * (pieces // 2), v * (pieces // 2)):
            part = jnp.einsum("gio,ok->gki", lax.dynamic_slice_in_dim(current3, start, pieces // 2, 0), diff, precision=FAST)
            for back3, ortho_t in zip(backs, orthos):
                inner = jnp.dot(ortho_t, diff, precision=HIGH)
                back_half = lax.dynamic_slice_in_dim(back3, start, pieces // 2, 0)
                part = part - 0.5 * jnp.einsum("lk,gli->gki", inner, back_half, precision=HIGH)
            halves.append(part)
        width = gram.shape[0]
        lanes = part.shape[2]
        tail = jnp.pad(gram.reshape(-1, lanes), ((0, 8 - width * width // lanes), (0, 0)))
        tail = jnp.broadcast_to(tail, (part.shape[0],) + tail.shape)
        halves = [jnp.concatenate([p, tail], axis=1) for p in halves]
        mixed, extra = halving_allreduce(halves[1], halves[0], axis, count, width)
        gram = extra[: width * width // lanes].reshape(width, width)
        lower = jnp.linalg.cholesky(0.5 * gram)
        inv = jax.scipy.linalg.solve_triangular(lower, eye, lower=True)
        back3 = jnp.einsum("kl,gli->gki", inv, mixed, precision=HIGH)
        ortho_t = jnp.dot(inv, diff.T, precision=HIGH)
        backs.append(back3)
        orthos.append(ortho_t)
        if step + 1 < STEPS:
            proj = jnp.einsum("gki,gil->kl", back3, factors3, precision=HIGH)
            side = side - 0.5 * lax.dot_general(ortho_t, proj, (((0,), (0,)), ((), ())), precision=HIGH)
    back_all = jnp.concatenate(backs, axis=1)
    back_all = jnp.transpose(back_all, (1, 0, 2)).reshape(back_all.shape[1], -1)
    ortho_all = jnp.concatenate(orthos)
    update = lax.dot_general(back_all, ortho_all, (((0,), (0,)), ((), ())), precision=FAST)
    new = current - 0.5 * update
    return (projected, new.astype(jnp.bfloat16)[None])


def solution(mesh):
    reps = mesh.shape["rep"]
    high = reps >> STEPS
    names = ("rh",) + tuple(f"b{s}" for s in reversed(range(STEPS)))
    devices = np.asarray(mesh.devices).reshape((high,) + (2,) * STEPS + (mesh.shape["tp"],))
    split = Mesh(devices, names + ("tp",))
    rep = names
    in_specs = (P(rep, "tp", None), P(rep, None, "tp"), P(rep, None, "tp"), P())
    out_specs = (P(rep, None, "tp"), P(rep, None, "tp"))
    return jax.shard_map(shards, mesh=split, in_specs=in_specs, out_specs=out_specs, check_vma=False)
```

```python
import numpy as np
import jax
import jax.numpy as jnp
from jax import lax
from jax.sharding import Mesh, PartitionSpec as P

D = 4096
STEPS = 3


HIGH = lax.Precision.HIGHEST
FAST = lax.Precision.HIGH
F32 = jnp.float32


def swap(block, axis):
    return lax.ppermute(block, axis, [(0, 1), (1, 0)])


def tp_perm(count, fn):
    return [(t, fn(t)) for t in range(count)]


def gather_tokens(own, count):
    if count != 8:
        whole = lax.all_gather(own, "tp", axis=0, tiled=False)
        return [whole[k] for k in range(count)], None
    nx = count // 2

    def shift(d):
        return tp_perm(count, lambda t: ((t // 2 + d) % nx) * 2 + t % 2)

    h = own.shape[0] // 2
    pair = tp_perm(count, lambda t: t ^ 1)
    a_y = lax.ppermute(own, "tp", pair)
    a_m = lax.ppermute(own, "tp", shift(1))
    a_p = lax.ppermute(own, "tp", shift(-1))
    b_m = lax.ppermute(a_y, "tp", shift(1))
    b_p = lax.ppermute(a_p, "tp", shift(-1))
    b_y = lax.ppermute(a_p, "tp", pair)
    c_y = lax.ppermute(b_p[:h], "tp", pair)
    c_p = lax.ppermute(b_y[h:], "tp", shift(-1))
    return [own, a_y, a_p, b_y, b_p, jnp.concatenate([c_y, c_p]), a_m, b_m], nx


def allreduce(parts, pair_axis, count):
    parts = [p + swap(p, pair_axis) for p in parts]
    bit = 1
    while bit < count:
        perm = tp_perm(count, lambda t, b=bit: t ^ b)
        parts = [p + lax.ppermute(p, "tp", perm) for p in parts]
        bit *= 2
    return parts


def halving_allreduce(keep, give, pair_axis, count):
    t = lax.axis_index("tp")
    stages = [(pair_axis, lax.axis_index(pair_axis), [(0, 1), (1, 0)])]
    bit = 1
    while bit < count:
        stages.append(("tp", (t // bit) % 2, tp_perm(count, lambda u, b=bit: u ^ b)))
        bit *= 2
    buf = keep + lax.ppermute(give, pair_axis, stages[0][2])
    for axis, v, perm in stages[1:]:
        half = buf.shape[0] // 2
        keep = lax.dynamic_slice_in_dim(buf, v * half, half, 0)
        give = lax.dynamic_slice_in_dim(buf, (1 - v) * half, half, 0)
        buf = keep + lax.ppermute(give, axis, perm)
    for axis, v, perm in reversed(stages):
        other = lax.ppermute(buf, axis, perm)
        buf = jnp.where(v == 1, jnp.concatenate([other, buf]), jnp.concatenate([buf, other]))
    return buf


def shards(acts, weights, cotangent, start_factors):
    scale = D ** (-0.5)
    count = lax.axis_size("tp")
    weight_part = weights[0]
    grad_out = cotangent[0]
    rows = acts.shape[1]
    blocks, nx = gather_tokens(acts[0], count)
    t = lax.axis_index("tp")
    if nx is None:
        order = jnp.arange(count)
    else:
        k = jnp.arange(count)
        order = ((t // 2 + k // 2) % nx) * 2 + ((t % 2) ^ (k % 2))
    grad_rel = jnp.take(grad_out.reshape(count, rows, -1), order, axis=0)
    groups = [(0, 1, 2, 6), (3, 4, 7), (5,)] if nx is not None else [tuple(range(count))]
    outs = [None] * count
    current = weight_part.astype(F32)
    side = lax.dot_general(weight_part.astype(F32), start_factors, (((0,), (0,)), ((), ())), precision=FAST)
    for group in groups:
        chunk = jnp.concatenate([blocks[k] for k in group])
        part = (jnp.dot(chunk, weight_part, preferred_element_type=F32) * scale).astype(jnp.bfloat16)
        for i, k in enumerate(group):
            outs[k] = part[i * rows:(i + 1) * rows]
        cot = jnp.concatenate([grad_rel[k] for k in group])
        term = lax.dot_general(chunk, cot, (((0,), (0,)), ((), ())), preferred_element_type=F32)
        current = current - 0.5 * scale * term
        lifted = jnp.dot(chunk, start_factors, precision=FAST)
        side = side - 0.5 * scale * lax.dot_general(cot, lifted, (((0,), (0,)), ((), ())), precision=FAST)
    out_rel = jnp.stack(outs)
    inverse = jnp.zeros((count,), jnp.int32).at[order].set(jnp.arange(count, dtype=jnp.int32))
    projected = jnp.take(out_rel, inverse, axis=0).reshape(count * rows, -1)[None]
    pieces = 2 * count
    current3 = current.reshape(pieces, -1, current.shape[1])
    factors3 = start_factors.reshape(pieces, -1, start_factors.shape[1])
    backs, orthos = [], []
    eye = jnp.eye(start_factors.shape[1], dtype=F32)
    for step in range(STEPS):
        axis = f"b{step}"
        diff = side - swap(side, axis)
        gram = jnp.dot(diff.T, diff, precision=HIGH)
        v = lax.axis_index(axis)
        halves = []
        for start in ((1 - v) * (pieces // 2), v * (pieces // 2)):
            part = jnp.einsum("gio,ok->gki", lax.dynamic_slice_in_dim(current3, start, pieces // 2, 0), diff, precision=FAST)
            for back3, ortho_t in zip(backs, orthos):
                inner = jnp.dot(ortho_t, diff, precision=HIGH)
                back_half = lax.dynamic_slice_in_dim(back3, start, pieces // 2, 0)
                part = part - 0.5 * jnp.einsum("lk,gli->gki", inner, back_half, precision=HIGH)
            halves.append(part)
        (gram,) = allreduce([gram], axis, count)
        mixed = halving_allreduce(halves[1], halves[0], axis, count)
        lower = jnp.linalg.cholesky(0.5 * gram)
        inv = jax.scipy.linalg.solve_triangular(lower, eye, lower=True)
        back3 = jnp.einsum("kl,gli->gki", inv, mixed, precision=HIGH)
        ortho_t = jnp.dot(inv, diff.T, precision=HIGH)
        backs.append(back3)
        orthos.append(ortho_t)
        if step + 1 < STEPS:
            proj = jnp.einsum("gki,gil->kl", back3, factors3, precision=HIGH)
            side = side - 0.5 * lax.dot_general(ortho_t, proj, (((0,), (0,)), ((), ())), precision=HIGH)
    back_all = jnp.concatenate(backs, axis=1)
    back_all = jnp.transpose(back_all, (1, 0, 2)).reshape(back_all.shape[1], -1)
    ortho_all = jnp.concatenate(orthos)
    update = lax.dot_general(back_all, ortho_all, (((0,), (0,)), ((), ())), precision=FAST)
    new = current - 0.5 * update
    return (projected, new.astype(jnp.bfloat16)[None])


def solution(mesh):
    reps = mesh.shape["rep"]
    high = reps >> STEPS
    names = ("rh",) + tuple(f"b{s}" for s in reversed(range(STEPS)))
    devices = np.asarray(mesh.devices).reshape((high,) + (2,) * STEPS + (mesh.shape["tp"],))
    split = Mesh(devices, names + ("tp",))
    rep = names
    in_specs = (P(rep, "tp", None), P(rep, None, "tp"), P(rep, None, "tp"), P())
    out_specs = (P(rep, None, "tp"), P(rep, None, "tp"))
    return jax.shard_map(shards, mesh=split, in_specs=in_specs, out_specs=out_specs, check_vma=False)
```

```python
import numpy as np
import jax
import jax.numpy as jnp
from jax import lax
from jax.sharding import Mesh, PartitionSpec as P

D = 4096
STEPS = 3


HIGH = lax.Precision.HIGHEST
FAST = lax.Precision.HIGH
F32 = jnp.float32


def swap(block, axis):
    return lax.ppermute(block, axis, [(0, 1), (1, 0)])


def tp_perm(count, fn):
    return [(t, fn(t)) for t in range(count)]


def gather_tokens(own, count):
    if count != 8:
        whole = lax.all_gather(own, "tp", axis=0, tiled=False)
        return [whole[k] for k in range(count)], None
    nx = count // 2

    def shift(d):
        return tp_perm(count, lambda t: ((t // 2 + d) % nx) * 2 + t % 2)

    h = own.shape[0] // 2
    pair = tp_perm(count, lambda t: t ^ 1)
    a_y = lax.ppermute(own, "tp", pair)
    a_m = lax.ppermute(own, "tp", shift(1))
    a_p = lax.ppermute(own, "tp", shift(-1))
    b_m = lax.ppermute(a_y, "tp", shift(1))
    b_p = lax.ppermute(a_p, "tp", shift(-1))
    b_y = lax.ppermute(a_p, "tp", pair)
    c_y = lax.ppermute(b_p[:h], "tp", pair)
    c_p = lax.ppermute(b_y[h:], "tp", shift(-1))
    return [own, a_y, a_p, b_y, b_p, jnp.concatenate([c_y, c_p]), a_m, b_m], nx


def allreduce(parts, pair_axis, count):
    parts = [p + swap(p, pair_axis) for p in parts]
    bit = 1
    while bit < count:
        perm = tp_perm(count, lambda t, b=bit: t ^ b)
        parts = [p + lax.ppermute(p, "tp", perm) for p in parts]
        bit *= 2
    return parts


def stages_of(pair_axis, count, pair_last):
    t = lax.axis_index("tp")
    stages = []
    bit = 1
    while bit < count:
        stages.append(("tp", (t // bit) % 2, tp_perm(count, lambda u, b=bit: u ^ b)))
        bit *= 2
    pair = (pair_axis, lax.axis_index(pair_axis), [(0, 1), (1, 0)])
    return stages + [pair] if pair_last else [pair] + stages


def halving_allreduce(keep, give, stages):
    buf = keep + lax.ppermute(give, stages[0][0], stages[0][2])
    for axis, v, perm in stages[1:]:
        half = buf.shape[0] // 2
        keep = lax.dynamic_slice_in_dim(buf, v * half, half, 0)
        give = lax.dynamic_slice_in_dim(buf, (1 - v) * half, half, 0)
        buf = keep + lax.ppermute(give, axis, perm)
    for axis, v, perm in reversed(stages):
        other = lax.ppermute(buf, axis, perm)
        buf = jnp.where(v == 1, jnp.concatenate([other, buf]), jnp.concatenate([buf, other]))
    return buf


def shards(acts, weights, cotangent, start_factors):
    scale = D ** (-0.5)
    count = lax.axis_size("tp")
    weight_part = weights[0]
    grad_out = cotangent[0]
    rows = acts.shape[1]
    blocks, nx = gather_tokens(acts[0], count)
    t = lax.axis_index("tp")
    if nx is None:
        order = jnp.arange(count)
    else:
        k = jnp.arange(count)
        order = ((t // 2 + k // 2) % nx) * 2 + ((t % 2) ^ (k % 2))
    grad_rel = jnp.take(grad_out.reshape(count, rows, -1), order, axis=0)
    groups = [(0, 1, 2, 6), (3, 4, 7), (5,)] if nx is not None else [tuple(range(count))]
    outs = [None] * count
    grad = None
    for group in groups:
        chunk = jnp.concatenate([blocks[k] for k in group])
        part = (jnp.dot(chunk, weight_part, preferred_element_type=F32) * scale).astype(jnp.bfloat16)
        for i, k in enumerate(group):
            outs[k] = part[i * rows:(i + 1) * rows]
        cot = jnp.concatenate([grad_rel[k] for k in group])
        term = lax.dot_general(chunk, cot, (((0,), (0,)), ((), ())), preferred_element_type=F32)
        grad = term if grad is None else grad + term
    out_rel = jnp.stack(outs)
    inverse = jnp.zeros((count,), jnp.int32).at[order].set(jnp.arange(count, dtype=jnp.int32))
    projected = jnp.take(out_rel, inverse, axis=0).reshape(count * rows, -1)[None]
    current = weight_part.astype(F32) - 0.5 * scale * grad
    side = lax.dot_general(current, start_factors, (((0,), (0,)), ((), ())), precision=FAST)
    pieces = 2 * count
    current3 = current.reshape(pieces, -1, current.shape[1])
    factors3 = start_factors.reshape(pieces, -1, start_factors.shape[1])
    backs, orthos = [], []
    eye = jnp.eye(start_factors.shape[1], dtype=F32)
    for step in range(STEPS):
        axis = f"b{step}"
        diff = side - swap(side, axis)
        gram = jnp.dot(diff.T, diff, precision=HIGH)
        stages = stages_of(axis, count, step == 1)
        v = stages[0][1]
        halves = []
        for start in ((1 - v) * (pieces // 2), v * (pieces // 2)):
            part = jnp.einsum("gio,ok->gki", lax.dynamic_slice_in_dim(current3, start, pieces // 2, 0), diff, precision=FAST)
            for back3, ortho_t in zip(backs, orthos):
                inner = jnp.dot(ortho_t, diff, precision=HIGH)
                back_half = lax.dynamic_slice_in_dim(back3, start, pieces // 2, 0)
                part = part - 0.5 * jnp.einsum("lk,gli->gki", inner, back_half, precision=HIGH)
            halves.append(part)
        (gram,) = allreduce([gram], axis, count)
        mixed = halving_allreduce(halves[1], halves[0], stages)
        lower = jnp.linalg.cholesky(0.5 * gram)
        inv = jax.scipy.linalg.solve_triangular(lower, eye, lower=True)
        back3 = jnp.einsum("kl,gli->gki", inv, mixed, precision=HIGH)
        ortho_t = jnp.dot(inv, diff.T, precision=HIGH)
        backs.append(back3)
        orthos.append(ortho_t)
        if step + 1 < STEPS:
            proj = jnp.einsum("gki,gil->kl", back3, factors3, precision=HIGH)
            side = side - 0.5 * lax.dot_general(ortho_t, proj, (((0,), (0,)), ((), ())), precision=HIGH)
    back_all = jnp.concatenate(backs, axis=1)
    back_all = jnp.transpose(back_all, (1, 0, 2)).reshape(back_all.shape[1], -1)
    ortho_all = jnp.concatenate(orthos)
    update = lax.dot_general(back_all, ortho_all, (((0,), (0,)), ((), ())), precision=FAST)
    new = current - 0.5 * update
    return (projected, new.astype(jnp.bfloat16)[None])


def solution(mesh):
    reps = mesh.shape["rep"]
    high = reps >> STEPS
    names = ("rh",) + tuple(f"b{s}" for s in reversed(range(STEPS)))
    devices = np.asarray(mesh.devices).reshape((high,) + (2,) * STEPS + (mesh.shape["tp"],))
    split = Mesh(devices, names + ("tp",))
    rep = names
    in_specs = (P(rep, "tp", None), P(rep, None, "tp"), P(rep, None, "tp"), P())
    out_specs = (P(rep, None, "tp"), P(rep, None, "tp"))
    return jax.shard_map(shards, mesh=split, in_specs=in_specs, out_specs=out_specs, check_vma=False)
```

```python
import numpy as np
import jax
import jax.numpy as jnp
from jax import lax
from jax.sharding import Mesh, PartitionSpec as P

D = 4096
STEPS = 3


HIGH = lax.Precision.HIGHEST
FAST = lax.Precision.HIGH
F32 = jnp.float32


def swap(block, axis):
    return lax.ppermute(block, axis, [(0, 1), (1, 0)])


def tp_perm(count, fn):
    return [(t, fn(t)) for t in range(count)]


def gather_tokens(own, count):
    if count != 8:
        whole = lax.all_gather(own, "tp", axis=0, tiled=False)
        return [whole[k] for k in range(count)], None
    nx = count // 2

    def shift(d):
        return tp_perm(count, lambda t: ((t // 2 + d) % nx) * 2 + t % 2)

    h = own.shape[0] // 2
    pair = tp_perm(count, lambda t: t ^ 1)
    a_y = lax.ppermute(own, "tp", pair)
    a_m = lax.ppermute(own, "tp", shift(1))
    a_p = lax.ppermute(own, "tp", shift(-1))
    b_m = lax.ppermute(a_y, "tp", shift(1))
    b_p = lax.ppermute(a_p, "tp", shift(-1))
    b_y = lax.ppermute(a_p, "tp", pair)
    c_y = lax.ppermute(b_p[:h], "tp", pair)
    c_p = lax.ppermute(b_y[h:], "tp", shift(-1))
    return [own, a_y, a_p, b_y, b_p, jnp.concatenate([c_y, c_p]), a_m, b_m], nx


def allreduce(parts, pair_axis, count):
    parts = [p + swap(p, pair_axis) for p in parts]
    bit = 1
    while bit < count:
        perm = tp_perm(count, lambda t, b=bit: t ^ b)
        parts = [p + lax.ppermute(p, "tp", perm) for p in parts]
        bit *= 2
    return parts


def halving_allreduce(keep, give, pair_axis, count):
    t = lax.axis_index("tp")
    stages = [(pair_axis, lax.axis_index(pair_axis), [(0, 1), (1, 0)])]
    bit = 1
    while bit < count:
        stages.append(("tp", (t // bit) % 2, tp_perm(count, lambda u, b=bit: u ^ b)))
        bit *= 2
    buf = keep + lax.ppermute(give, pair_axis, stages[0][2])
    for axis, v, perm in stages[1:]:
        half = buf.shape[0] // 2
        keep = lax.dynamic_slice_in_dim(buf, v * half, half, 0)
        give = lax.dynamic_slice_in_dim(buf, (1 - v) * half, half, 0)
        buf = keep + lax.ppermute(give, axis, perm)
    for axis, v, perm in reversed(stages):
        other = lax.ppermute(buf, axis, perm)
        buf = jnp.where(v == 1, jnp.concatenate([other, buf]), jnp.concatenate([buf, other]))
    return buf


def shards(acts, weights, cotangent, start_factors):
    scale = D ** (-0.5)
    count = lax.axis_size("tp")
    weight_part = weights[0]
    grad_out = cotangent[0]
    rows = acts.shape[1]
    blocks, nx = gather_tokens(acts[0], count)
    t = lax.axis_index("tp")
    if nx is None:
        order = jnp.arange(count)
    else:
        k = jnp.arange(count)
        order = ((t // 2 + k // 2) % nx) * 2 + ((t % 2) ^ (k % 2))
    grad_rel = jnp.take(grad_out.reshape(count, rows, -1), order, axis=0)
    groups = [(0, 1, 2, 6), (3, 4, 7), (5,)] if nx is not None else [tuple(range(count))]
    outs = [None] * count
    grad = None
    for group in groups:
        chunk = jnp.concatenate([blocks[k] for k in group])
        part = (jnp.dot(chunk, weight_part, preferred_element_type=F32) * scale).astype(jnp.bfloat16)
        for i, k in enumerate(group):
            outs[k] = part[i * rows:(i + 1) * rows]
        cot = jnp.concatenate([grad_rel[k] for k in group])
        term = lax.dot_general(chunk, cot, (((0,), (0,)), ((), ())), preferred_element_type=F32)
        grad = term if grad is None else grad + term
    out_rel = jnp.stack(outs)
    inverse = jnp.zeros((count,), jnp.int32).at[order].set(jnp.arange(count, dtype=jnp.int32))
    projected = jnp.take(out_rel, inverse, axis=0).reshape(count * rows, -1)[None]
    current = weight_part.astype(F32) - 0.5 * scale * grad
    side = lax.dot_general(current, start_factors, (((0,), (0,)), ((), ())), precision=FAST)
    pieces = 2 * count
    current3 = current.reshape(pieces, -1, current.shape[1])
    factors3 = start_factors.reshape(pieces, -1, start_factors.shape[1])
    backs, orthos = [], []
    eye = jnp.eye(start_factors.shape[1], dtype=F32)
    for step in range(STEPS):
        axis = f"b{step}"
        diff = side - swap(side, axis)
        gram = jnp.dot(diff.T, diff, precision=FAST)
        v = lax.axis_index(axis)
        halves = []
        for start in ((1 - v) * (pieces // 2), v * (pieces // 2)):
            part = jnp.einsum("gio,ok->gki", lax.dynamic_slice_in_dim(current3, start, pieces // 2, 0), diff, precision=FAST)
            for back3, ortho_t in zip(backs, orthos):
                inner = jnp.dot(ortho_t, diff, precision=FAST)
                back_half = lax.dynamic_slice_in_dim(back3, start, pieces // 2, 0)
                part = part - 0.5 * jnp.einsum("lk,gli->gki", inner, back_half, precision=FAST)
            halves.append(part)
        (gram,) = allreduce([gram], axis, count)
        mixed = halving_allreduce(halves[1], halves[0], axis, count)
        lower = jnp.linalg.cholesky(0.5 * gram)
        inv = jax.scipy.linalg.solve_triangular(lower, eye, lower=True)
        back3 = jnp.einsum("kl,gli->gki", inv, mixed, precision=FAST)
        ortho_t = jnp.dot(inv, diff.T, precision=FAST)
        backs.append(back3)
        orthos.append(ortho_t)
        if step + 1 < STEPS:
            proj = jnp.einsum("gki,gil->kl", back3, factors3, precision=FAST)
            side = side - 0.5 * lax.dot_general(ortho_t, proj, (((0,), (0,)), ((), ())), precision=FAST)
    back_all = jnp.concatenate(backs, axis=1)
    back_all = jnp.transpose(back_all, (1, 0, 2)).reshape(back_all.shape[1], -1)
    ortho_all = jnp.concatenate(orthos)
    update = lax.dot_general(back_all, ortho_all, (((0,), (0,)), ((), ())), precision=FAST)
    new = current - 0.5 * update
    return (projected, new.astype(jnp.bfloat16)[None])


def solution(mesh):
    reps = mesh.shape["rep"]
    high = reps >> STEPS
    names = ("rh",) + tuple(f"b{s}" for s in reversed(range(STEPS)))
    devices = np.asarray(mesh.devices).reshape((high,) + (2,) * STEPS + (mesh.shape["tp"],))
    split = Mesh(devices, names + ("tp",))
    rep = names
    in_specs = (P(rep, "tp", None), P(rep, None, "tp"), P(rep, None, "tp"), P())
    out_specs = (P(rep, None, "tp"), P(rep, None, "tp"))
    return jax.shard_map(shards, mesh=split, in_specs=in_specs, out_specs=out_specs, check_vma=False)
```

```python
import numpy as np
import jax
import jax.numpy as jnp
from jax import lax
from jax.sharding import Mesh, PartitionSpec as P

D = 4096
STEPS = 3


HIGH = lax.Precision.HIGHEST
FAST = lax.Precision.HIGH
F32 = jnp.float32


def swap(block, axis):
    return lax.ppermute(block, axis, [(0, 1), (1, 0)])


def tp_perm(count, fn):
    return [(t, fn(t)) for t in range(count)]


def gather_tokens(own, count):
    if count != 8:
        whole = lax.all_gather(own, "tp", axis=0, tiled=False)
        return [whole[k] for k in range(count)], None
    nx = count // 2

    def shift(d):
        return tp_perm(count, lambda t: ((t // 2 + d) % nx) * 2 + t % 2)

    h = own.shape[0] // 2
    pair = tp_perm(count, lambda t: t ^ 1)
    a_y = lax.ppermute(own, "tp", pair)
    a_m = lax.ppermute(own, "tp", shift(1))
    a_p = lax.ppermute(own, "tp", shift(-1))
    b_m = lax.ppermute(a_y, "tp", shift(1))
    b_p = lax.ppermute(a_p, "tp", shift(-1))
    b_y = lax.ppermute(a_p, "tp", pair)
    cut = [0, 3 * h // 4, 3 * h // 2, 2 * h]
    c_y = lax.ppermute(b_p[cut[0]:cut[1]], "tp", pair)
    c_p = lax.ppermute(b_y[cut[1]:cut[2]], "tp", shift(-1))
    c_m = lax.ppermute(b_m[cut[2]:cut[3]], "tp", shift(1))
    return [own, a_y, a_p, b_y, b_p, jnp.concatenate([c_y, c_p, c_m]), a_m, b_m], nx


def allreduce(parts, pair_axis, count):
    parts = [p + swap(p, pair_axis) for p in parts]
    bit = 1
    while bit < count:
        perm = tp_perm(count, lambda t, b=bit: t ^ b)
        parts = [p + lax.ppermute(p, "tp", perm) for p in parts]
        bit *= 2
    return parts


def halving_allreduce(keep, give, pair_axis, count):
    t = lax.axis_index("tp")
    stages = [(pair_axis, lax.axis_index(pair_axis), [(0, 1), (1, 0)])]
    bit = 1
    while bit < count:
        stages.append(("tp", (t // bit) % 2, tp_perm(count, lambda u, b=bit: u ^ b)))
        bit *= 2
    buf = keep + lax.ppermute(give, pair_axis, stages[0][2])
    for axis, v, perm in stages[1:]:
        half = buf.shape[0] // 2
        keep = lax.dynamic_slice_in_dim(buf, v * half, half, 0)
        give = lax.dynamic_slice_in_dim(buf, (1 - v) * half, half, 0)
        buf = keep + lax.ppermute(give, axis, perm)
    for axis, v, perm in reversed(stages):
        other = lax.ppermute(buf, axis, perm)
        buf = jnp.where(v == 1, jnp.concatenate([other, buf]), jnp.concatenate([buf, other]))
    return buf


def shards(acts, weights, cotangent, start_factors):
    scale = D ** (-0.5)
    count = lax.axis_size("tp")
    weight_part = weights[0]
    grad_out = cotangent[0]
    rows = acts.shape[1]
    blocks, nx = gather_tokens(acts[0], count)
    t = lax.axis_index("tp")
    if nx is None:
        order = jnp.arange(count)
    else:
        k = jnp.arange(count)
        order = ((t // 2 + k // 2) % nx) * 2 + ((t % 2) ^ (k % 2))
    grad_rel = jnp.take(grad_out.reshape(count, rows, -1), order, axis=0)
    groups = [(0, 1, 2, 6), (3, 4, 7), (5,)] if nx is not None else [tuple(range(count))]
    outs = [None] * count
    grad = None
    for group in groups:
        chunk = jnp.concatenate([blocks[k] for k in group])
        part = (jnp.dot(chunk, weight_part, preferred_element_type=F32) * scale).astype(jnp.bfloat16)
        for i, k in enumerate(group):
            outs[k] = part[i * rows:(i + 1) * rows]
        cot = jnp.concatenate([grad_rel[k] for k in group])
        term = lax.dot_general(chunk, cot, (((0,), (0,)), ((), ())), preferred_element_type=F32)
        grad = term if grad is None else grad + term
    out_rel = jnp.stack(outs)
    inverse = jnp.zeros((count,), jnp.int32).at[order].set(jnp.arange(count, dtype=jnp.int32))
    projected = jnp.take(out_rel, inverse, axis=0).reshape(count * rows, -1)[None]
    current = weight_part.astype(F32) - 0.5 * scale * grad
    side = lax.dot_general(current, start_factors, (((0,), (0,)), ((), ())), precision=FAST)
    pieces = 2 * count
    current3 = current.reshape(pieces, -1, current.shape[1])
    factors3 = start_factors.reshape(pieces, -1, start_factors.shape[1])
    backs, orthos = [], []
    eye = jnp.eye(start_factors.shape[1], dtype=F32)
    for step in range(STEPS):
        axis = f"b{step}"
        diff = side - swap(side, axis)
        gram = jnp.dot(diff.T, diff, precision=FAST)
        v = lax.axis_index(axis)
        halves = []
        for start in ((1 - v) * (pieces // 2), v * (pieces // 2)):
            part = jnp.einsum("gio,ok->gki", lax.dynamic_slice_in_dim(current3, start, pieces // 2, 0), diff, precision=FAST)
            for back3, ortho_t in zip(backs, orthos):
                inner = jnp.dot(ortho_t, diff, precision=FAST)
                back_half = lax.dynamic_slice_in_dim(back3, start, pieces // 2, 0)
                part = part - 0.5 * jnp.einsum("lk,gli->gki", inner, back_half, precision=FAST)
            halves.append(part)
        (gram,) = allreduce([gram], axis, count)
        mixed = halving_allreduce(halves[1], halves[0], axis, count)
        lower = jnp.linalg.cholesky(0.5 * gram)
        inv = jax.scipy.linalg.solve_triangular(lower, eye, lower=True)
        back3 = jnp.einsum("kl,gli->gki", inv, mixed, precision=FAST)
        ortho_t = jnp.dot(inv, diff.T, precision=FAST)
        backs.append(back3)
        orthos.append(ortho_t)
        if step + 1 < STEPS:
            proj = jnp.einsum("gki,gil->kl", back3, factors3, precision=FAST)
            side = side - 0.5 * lax.dot_general(ortho_t, proj, (((0,), (0,)), ((), ())), precision=FAST)
    back_all = jnp.concatenate(backs, axis=1)
    back_all = jnp.transpose(back_all, (1, 0, 2)).reshape(back_all.shape[1], -1)
    ortho_all = jnp.concatenate(orthos)
    update = lax.dot_general(back_all, ortho_all, (((0,), (0,)), ((), ())), precision=FAST)
    new = current - 0.5 * update
    return (projected, new.astype(jnp.bfloat16)[None])


def solution(mesh):
    reps = mesh.shape["rep"]
    high = reps >> STEPS
    names = ("rh",) + tuple(f"b{s}" for s in reversed(range(STEPS)))
    devices = np.asarray(mesh.devices).reshape((high,) + (2,) * STEPS + (mesh.shape["tp"],))
    split = Mesh(devices, names + ("tp",))
    rep = names
    in_specs = (P(rep, "tp", None), P(rep, None, "tp"), P(rep, None, "tp"), P())
    out_specs = (P(rep, None, "tp"), P(rep, None, "tp"))
    return jax.shard_map(shards, mesh=split, in_specs=in_specs, out_specs=out_specs, check_vma=False)
```

```python
import numpy as np
import jax
import jax.numpy as jnp
from jax import lax
from jax.sharding import Mesh, PartitionSpec as P

D = 4096
STEPS = 3


HIGH = lax.Precision.HIGHEST
FAST = lax.Precision.HIGH
F32 = jnp.float32


def swap(block, axis):
    return lax.ppermute(block, axis, [(0, 1), (1, 0)])


def tp_perm(count, fn):
    return [(t, fn(t)) for t in range(count)]


def gather_tokens(own, count):
    if count != 8:
        whole = lax.all_gather(own, "tp", axis=0, tiled=False)
        return [whole[k] for k in range(count)], None
    nx = count // 2

    def shift(d):
        return tp_perm(count, lambda t: ((t // 2 + d) % nx) * 2 + t % 2)

    h = own.shape[0] // 2
    pair = tp_perm(count, lambda t: t ^ 1)
    a_y = lax.ppermute(own, "tp", pair)
    a_m = lax.ppermute(own, "tp", shift(1))
    a_p = lax.ppermute(own, "tp", shift(-1))
    b_m = lax.ppermute(a_y, "tp", shift(1))
    b_p = lax.ppermute(a_p, "tp", shift(-1))
    b_y = lax.ppermute(a_p, "tp", pair)
    cut = [0, 3 * h // 4, 3 * h // 2, 2 * h]
    c_y = lax.ppermute(b_p[cut[0]:cut[1]], "tp", pair)
    c_p = lax.ppermute(b_y[cut[1]:cut[2]], "tp", shift(-1))
    c_m = lax.ppermute(b_m[cut[2]:cut[3]], "tp", shift(1))
    return [own, a_y, a_p, b_y, b_p, jnp.concatenate([c_y, c_p, c_m]), a_m, b_m], nx


def allreduce(parts, pair_axis, count):
    parts = [p + swap(p, pair_axis) for p in parts]
    bit = 1
    while bit < count:
        perm = tp_perm(count, lambda t, b=bit: t ^ b)
        parts = [p + lax.ppermute(p, "tp", perm) for p in parts]
        bit *= 2
    return parts


def halving_allreduce(keep, give, pair_axis, count):
    t = lax.axis_index("tp")
    stages = [(pair_axis, lax.axis_index(pair_axis), [(0, 1), (1, 0)])]
    bit = 1
    while bit < count:
        stages.append(("tp", (t // bit) % 2, tp_perm(count, lambda u, b=bit: u ^ b)))
        bit *= 2
    buf = keep + lax.ppermute(give, pair_axis, stages[0][2])
    for axis, v, perm in stages[1:]:
        half = buf.shape[0] // 2
        keep = lax.dynamic_slice_in_dim(buf, v * half, half, 0)
        give = lax.dynamic_slice_in_dim(buf, (1 - v) * half, half, 0)
        buf = keep + lax.ppermute(give, axis, perm)
    for axis, v, perm in reversed(stages):
        other = lax.ppermute(buf, axis, perm)
        buf = jnp.where(v == 1, jnp.concatenate([other, buf]), jnp.concatenate([buf, other]))
    return buf


def shards(acts, weights, cotangent, start_factors):
    scale = D ** (-0.5)
    count = lax.axis_size("tp")
    weight_part = weights[0]
    grad_out = cotangent[0]
    rows = acts.shape[1]
    blocks, nx = gather_tokens(acts[0], count)
    t = lax.axis_index("tp")
    if nx is None:
        order = jnp.arange(count)
    else:
        k = jnp.arange(count)
        order = ((t // 2 + k // 2) % nx) * 2 + ((t % 2) ^ (k % 2))
    grad_rel = jnp.take(grad_out.reshape(count, rows, -1), order, axis=0)
    groups = [(0, 1, 2, 6), (3, 4, 7), (5,)] if nx is not None else [tuple(range(count))]
    outs = [None] * count
    current = weight_part.astype(F32)
    for group in groups:
        chunk = jnp.concatenate([blocks[k] for k in group])
        part = (jnp.dot(chunk, weight_part, preferred_element_type=F32) * scale).astype(jnp.bfloat16)
        for i, k in enumerate(group):
            outs[k] = part[i * rows:(i + 1) * rows]
        cot = jnp.concatenate([grad_rel[k] for k in group])
        term = lax.dot_general(chunk, cot, (((0,), (0,)), ((), ())), preferred_element_type=F32)
        current = current - 0.5 * scale * term
    out_rel = jnp.stack(outs)
    inverse = jnp.zeros((count,), jnp.int32).at[order].set(jnp.arange(count, dtype=jnp.int32))
    projected = jnp.take(out_rel, inverse, axis=0).reshape(count * rows, -1)[None]
    side = lax.dot_general(current, start_factors, (((0,), (0,)), ((), ())), precision=FAST)
    pieces = 2 * count
    current3 = current.reshape(pieces, -1, current.shape[1])
    factors3 = start_factors.reshape(pieces, -1, start_factors.shape[1])
    backs, orthos = [], []
    eye = jnp.eye(start_factors.shape[1], dtype=F32)
    for step in range(STEPS):
        axis = f"b{step}"
        diff = side - swap(side, axis)
        gram = jnp.dot(diff.T, diff, precision=FAST)
        v = lax.axis_index(axis)
        halves = []
        for start in ((1 - v) * (pieces // 2), v * (pieces // 2)):
            part = jnp.einsum("gio,ok->gki", lax.dynamic_slice_in_dim(current3, start, pieces // 2, 0), diff, precision=FAST)
            for back3, ortho_t in zip(backs, orthos):
                inner = jnp.dot(ortho_t, diff, precision=FAST)
                back_half = lax.dynamic_slice_in_dim(back3, start, pieces // 2, 0)
                part = part - 0.5 * jnp.einsum("lk,gli->gki", inner, back_half, precision=FAST)
            halves.append(part)
        (gram,) = allreduce([gram], axis, count)
        mixed = halving_allreduce(halves[1], halves[0], axis, count)
        lower = jnp.linalg.cholesky(0.5 * gram)
        inv = jax.scipy.linalg.solve_triangular(lower, eye, lower=True)
        back3 = jnp.einsum("kl,gli->gki", inv, mixed, precision=FAST)
        ortho_t = jnp.dot(inv, diff.T, precision=FAST)
        backs.append(back3)
        orthos.append(ortho_t)
        if step + 1 < STEPS:
            proj = jnp.einsum("gki,gil->kl", back3, factors3, precision=FAST)
            side = side - 0.5 * lax.dot_general(ortho_t, proj, (((0,), (0,)), ((), ())), precision=FAST)
    back_all = jnp.concatenate(backs, axis=1)
    back_all = jnp.transpose(back_all, (1, 0, 2)).reshape(back_all.shape[1], -1)
    ortho_all = jnp.concatenate(orthos)
    update = lax.dot_general(back_all, ortho_all, (((0,), (0,)), ((), ())), precision=FAST)
    new = current - 0.5 * update
    return (projected, new.astype(jnp.bfloat16)[None])


def solution(mesh):
    reps = mesh.shape["rep"]
    high = reps >> STEPS
    names = ("rh",) + tuple(f"b{s}" for s in reversed(range(STEPS)))
    devices = np.asarray(mesh.devices).reshape((high,) + (2,) * STEPS + (mesh.shape["tp"],))
    split = Mesh(devices, names + ("tp",))
    rep = names
    in_specs = (P(rep, "tp", None), P(rep, None, "tp"), P(rep, None, "tp"), P())
    out_specs = (P(rep, None, "tp"), P(rep, None, "tp"))
    return jax.shard_map(shards, mesh=split, in_specs=in_specs, out_specs=out_specs, check_vma=False)
```
